256 devices in a mesh: section: 4 (over x), shard: 16 (over z, core), tensor: 4 (over y).
Axes of the slice: x: 4, y: 4, z: 8, core: 2. Of those that a mesh axis runs over, the one named last changes fastest.
Arguments:
- grad_terms: float32 [4, 16, 5120, 1280], P('section', 'shard', 'tensor'), may hold values from -5 to 5
- weights: bfloat16 [4, 4, 1280, 1280], P('section', 'tensor', 'shard'), may hold values from -4 to 4
- basis: float32 [4, 1280, 256], P('section'), may hold values from -5 to 5
- first_moment: float32 [4, 4, 1280, 256], P('section', 'tensor', 'shard'), may hold values from -4 to 4
- second_moment: float32 [4, 4, 1280, 256], P('section', 'tensor', 'shard'), may hold values from 0.1 to 2
Outputs:
- new_weights: bfloat16 [4, 4, 1280, 1280], P('section', 'tensor', 'shard')
- new_first: float32 [4, 4, 1280, 256], P('section', 'tensor', 'shard')
- new_second: float32 [4, 4, 1280, 256], P('section', 'tensor', 'shard')
- new_basis: float32 [4, 1280, 256], P('section')
The draws below stay inside these ranges and needn't reach their ends.
All inputs are finite; a program needn't handle non-finite values.
Results may differ from the reference program's by a relative error of at most 0.001.
Values sent between devices are 32-bit elements; how exact they have to be, the bound alone decides.
No kernel may reach another device: no remote copies, remote signals or barrier semaphores. Data moves between devices by JAX's collectives and lax.ppermute only.
A program may use at most 64 MiB of HBM per device.

```python
import math
import jax
import jax.numpy as jnp
from jax import lax

D = 1280
FF = 5120
R = 256
NS_STEPS = 5
LAYERS = 4
N_SHARD = 16
N_TENSOR = 4


def strengthened(entries, own_key, source, target, shards_of, factor):
    def block_of(axis_at):
        return (jnp.arange(entries.shape[axis_at]) // (entries.shape[axis_at] // shards_of)).reshape((-1,) + (1,) * (entries.ndim - 1 - axis_at))

    near = jax.random.permutation(own_key, shards_of)[block_of(target)]
    second = (block_of(target) + shards_of // 2) % shards_of
    return jnp.where((block_of(source) == near) | (block_of(source) == second), factor * entries, entries)


def block_levels(stream_key, shape, shards, low, high):
    gain, own = 1.0, jax.random.fold_in(stream_key, 6)
    for position, blocks in shards:
        draws = jnp.exp(jax.random.uniform(jax.random.fold_in(own, position), (blocks,), jnp.float32, low / len(shards), high / len(shards)))
        gain = gain * jnp.repeat(draws, shape[position] // blocks).reshape([-1 if axis == position else 1 for axis in range(len(shape))])
    return gain


def gaussian(stream_key, extent, scale, most, cuts=(), dtype=jnp.bfloat16):
    entries = scale * jax.random.normal(stream_key, extent, jnp.float32)
    if cuts:
        entries = entries * block_levels(stream_key, extent, cuts, -0.22, 0.18)
    return jnp.clip(entries, -most, most).astype(dtype)


def bell_draw_with(key, extent, spread, reach, shards, heavy, dtype=jnp.bfloat16):
    drawn = spread * jax.random.normal(key, extent, jnp.float32)
    if shards:
        drawn = drawn * block_levels(key, extent, shards, -0.22, 0.18)
    return jnp.clip(strengthened(drawn, jax.random.fold_in(key, 3), *heavy), -reach, reach).astype(dtype)


def setup_inputs(seed: int = 0) -> dict:
    keys = jax.random.split(jax.random.key(seed), 6)
    return {
        "grad_terms": bell_draw_with(keys[0], (LAYERS, N_SHARD, FF, D), 0.25, 5.0, ((0, 4), (1, 16), (2, 4)), (1, 2, 16, 2.0), jnp.float32),
        "weights": gaussian(keys[1], (LAYERS, N_TENSOR, FF // N_TENSOR, D), 1.0, 4.0, ((0, 4), (1, 4), (2, 16))),
        "basis": gaussian(keys[2], (LAYERS, D, R), 1.0, 5.0, ((0, 4),), jnp.float32),
        "first_moment": gaussian(keys[3], (LAYERS, N_TENSOR, FF // N_TENSOR, R), 0.5, 4.0, ((0, 4), (1, 4), (2, 16)), jnp.float32),
        "second_moment": jnp.clip(jnp.exp(math.log(2.0) - 2.9957323 * jax.random.uniform(keys[4], (LAYERS, N_TENSOR, FF // N_TENSOR, R), jnp.float32) ** block_levels(keys[4], (LAYERS, N_TENSOR, FF // N_TENSOR, R), ((0, 4), (1, 4), (2, 16)), -0.2, 0.2)), 0.1, 2.0),
    }


def matmul(left, right):
    return jnp.dot(left, right, precision=lax.Precision.HIGHEST, preferred_element_type=jnp.float32)

def inner_rows(left, right):
    return lax.dot_general(left, right, (((0,), (0,)), ((), ())), precision=lax.Precision.HIGHEST, preferred_element_type=jnp.float32)

def local_gram(iterate):
    return inner_rows(iterate, iterate)

def newton_steps(power):
    gram_now = local_gram(power)
    scaling = lax.rsqrt(jnp.trace(gram_now) + 1e-06)
    iterate = power * scaling
    gram_now = gram_now * (scaling * scaling)
    for sweep in range(NS_STEPS):
        iterate = 1.5 * iterate - 0.5 * matmul(iterate, gram_now)
        if sweep + 1 < NS_STEPS:
            gram_now = local_gram(iterate)
    return iterate

def reference(grad_terms, weights, basis, first_moment, second_moment):
    root_width = math.sqrt(D)
    weight_list, first_list, second_list, basis_list = ([], [], [], [])
    for layer in range(LAYERS):
        gradient = lax.optimization_barrier(jnp.sum(grad_terms[layer], axis=0))
        basis_now = basis[layer]
        low_rank = matmul(gradient, basis_now) / root_width
        moment_one = 0.9 * first_moment[layer].reshape(FF, R) + 0.1 * low_rank
        moment_two = 0.95 * second_moment[layer].reshape(FF, R) + 0.05 * low_rank * low_rank
        direction = moment_one / (jnp.sqrt(moment_two) + 1e-08)
        update = lax.dot_general(direction, basis_now, (((1,), (1,)), ((), ())), precision=lax.Precision.HIGHEST, preferred_element_type=jnp.float32)
        stepped = weights[layer].reshape(FF, D).astype(jnp.float32) - 0.5 * update / root_width
        normed = stepped * lax.rsqrt(lax.optimization_barrier(jnp.mean(stepped * stepped, axis=1, keepdims=True)) + 1e-06)
        power = inner_rows(gradient, low_rank)
        iterate = newton_steps(power)
        weight_list.append(normed.astype(jnp.bfloat16).reshape(N_TENSOR, FF // N_TENSOR, D))
        first_list.append(moment_one.reshape(N_TENSOR, FF // N_TENSOR, R))
        second_list.append(moment_two.reshape(N_TENSOR, FF // N_TENSOR, R))
        basis_list.append(iterate * root_width)
    return (jnp.stack(weight_list), jnp.stack(first_list), jnp.stack(second_list), jnp.stack(basis_list))
```

```python
import math

import jax
import jax.numpy as jnp
from jax import lax
from jax.sharding import PartitionSpec as P

NS_STEPS = 5


def matmul(left, right):
    return jnp.dot(left, right, precision=lax.Precision.HIGHEST, preferred_element_type=jnp.float32)


def inner_rows(left, right):
    return lax.dot_general(
        left,
        right,
        (((0,), (0,)), ((), ())),
        precision=lax.Precision.HIGHEST,
        preferred_element_type=jnp.float32,
    )


def local_gram(iterate):
    return inner_rows(iterate, iterate)


def newton_steps(power_part, gram_fn):
    gram_now = gram_fn(power_part)
    scaling = lax.rsqrt(jnp.trace(gram_now) + 1e-06)
    iterate = power_part * scaling
    gram_now = gram_now * (scaling * scaling)
    for sweep in range(NS_STEPS):
        iterate = 1.5 * iterate - 0.5 * matmul(iterate, gram_now)
        if sweep + 1 < NS_STEPS:
            gram_now = gram_fn(iterate)
    return iterate


def per_device(grad_terms, weights, basis, first_moment, second_moment):
    gradient = grad_terms[0, 0]
    basis_now = basis[0]
    root_width = math.sqrt(basis_now.shape[0])
    rows = first_moment.shape[2]
    low_rank = lax.psum_scatter(matmul(gradient, basis_now), "shard", scatter_dimension=0, tiled=True) / root_width
    low_rank_block = lax.all_gather(low_rank, "shard", axis=0, tiled=True)
    power_part = inner_rows(gradient, low_rank_block)
    flat = power_part.reshape(-1, 640)
    power_rows = lax.psum_scatter(flat, "shard", scatter_dimension=0, tiled=True)
    power_rows = lax.psum_scatter(power_rows, "tensor", scatter_dimension=0, tiled=True)
    power_rows = lax.all_gather(power_rows, "tensor", axis=0, tiled=True)
    power = lax.all_gather(power_rows, "shard", axis=0, tiled=True).reshape(power_part.shape)
    moment_one = 0.9 * first_moment[0, 0] + 0.1 * low_rank
    moment_two = 0.95 * second_moment[0, 0] + 0.05 * low_rank * low_rank
    direction = moment_one / (jnp.sqrt(moment_two) + 1e-08)
    update = lax.dot_general(
        direction,
        basis_now,
        (((1,), (1,)), ((), ())),
        precision=lax.Precision.HIGHEST,
        preferred_element_type=jnp.float32,
    )
    stepped = weights[0, 0].astype(jnp.float32) - 0.5 * update / root_width
    normed = stepped * lax.rsqrt(jnp.mean(stepped * stepped, axis=1, keepdims=True) + 1e-06)
    new_weights = normed.astype(jnp.bfloat16)
    iterate = newton_steps(power, local_gram)
    new_basis = iterate * root_width
    return (
        new_weights[None, None],
        moment_one[None, None],
        moment_two[None, None],
        new_basis[None],
    )


def solution(mesh):
    return jax.shard_map(
        per_device,
        mesh=mesh,
        in_specs=(
            P("section", "shard", "tensor", None),
            P("section", "tensor", "shard", None),
            P("section", None, None),
            P("section", "tensor", "shard", None),
            P("section", "tensor", "shard", None),
        ),
        out_specs=(
            P("section", "tensor", "shard", None),
            P("section", "tensor", "shard", None),
            P("section", "tensor", "shard", None),
            P("section", None, None),
        ),
        check_vma=False,
    )
```

```python
import math

import jax
import jax.numpy as jnp
from jax import lax
from jax.sharding import Mesh, PartitionSpec as P

NS_STEPS = 5


def matmul(left, right):
    return jnp.dot(left, right, precision=lax.Precision.HIGHEST, preferred_element_type=jnp.float32)


def inner_rows(left, right):
    return lax.dot_general(
        left,
        right,
        (((0,), (0,)), ((), ())),
        precision=lax.Precision.HIGHEST,
        preferred_element_type=jnp.float32,
    )


def local_gram(iterate):
    return inner_rows(iterate, iterate)


def newton_steps(power_part, gram_fn):
    gram_now = gram_fn(power_part)
    scaling = lax.rsqrt(jnp.trace(gram_now) + 1e-06)
    iterate = power_part * scaling
    gram_now = gram_now * (scaling * scaling)
    for sweep in range(NS_STEPS):
        iterate = 1.5 * iterate - 0.5 * matmul(iterate, gram_now)
        if sweep + 1 < NS_STEPS:
            gram_now = gram_fn(iterate)
    return iterate


def swap_cores(x):
    return lax.ppermute(x, "core", [(0, 1), (1, 0)])


def place_halves(own, partner, core):
    first = jnp.where(core == 0, own, partner)
    second = jnp.where(core == 0, partner, own)
    return jnp.stack([first, second])


def per_device(grad_terms, weights, basis, first_moment, second_moment):
    gradient = grad_terms[0, 0]
    basis_now = basis[0]
    root_width = math.sqrt(basis_now.shape[0])
    rows = first_moment.shape[2]
    n_z = lax.axis_size("z")
    core = lax.axis_index("core")
    partial = matmul(gradient, basis_now).reshape(n_z, 2, rows, -1)
    own = lax.dynamic_index_in_dim(partial, core, axis=1, keepdims=False)
    other = lax.dynamic_index_in_dim(partial, 1 - core, axis=1, keepdims=False)
    chip_sum = own + swap_cores(other)
    low_rank = lax.all_to_all(chip_sum, "z", 0, 0, tiled=True).sum(axis=0) / root_width
    gathered = lax.all_to_all(jnp.broadcast_to(low_rank[None], (n_z,) + low_rank.shape), "z", 0, 0, tiled=True)
    low_rank_block = place_halves(gathered, swap_cores(gathered), core)
    low_rank_block = jnp.moveaxis(low_rank_block, 0, 1).reshape(gradient.shape[0], -1)
    power_part = inner_rows(gradient, low_rank_block)
    n_group = n_z * lax.axis_size("tensor")
    halves = power_part.reshape(2, n_group, -1, power_part.shape[1])
    own_half = lax.dynamic_index_in_dim(halves, core, axis=0, keepdims=False)
    other_half = lax.dynamic_index_in_dim(halves, 1 - core, axis=0, keepdims=False)
    chip_half = own_half + swap_cores(other_half)
    piece = lax.all_to_all(chip_half, ("z", "tensor"), 0, 0, tiled=True).sum(axis=0)
    half = lax.all_to_all(jnp.broadcast_to(piece[None], chip_half.shape), ("z", "tensor"), 0, 0, tiled=True)
    power = place_halves(half, swap_cores(half), core).reshape(power_part.shape)
    moment_one = 0.9 * first_moment[0, 0] + 0.1 * low_rank
    moment_two = 0.95 * second_moment[0, 0] + 0.05 * low_rank * low_rank
    direction = moment_one / (jnp.sqrt(moment_two) + 1e-08)
    update = lax.dot_general(
        direction,
        basis_now,
        (((1,), (1,)), ((), ())),
        precision=lax.Precision.HIGHEST,
        preferred_element_type=jnp.float32,
    )
    stepped = weights[0, 0].astype(jnp.float32) - 0.5 * update / root_width
    normed = stepped * lax.rsqrt(jnp.mean(stepped * stepped, axis=1, keepdims=True) + 1e-06)
    new_weights = normed.astype(jnp.bfloat16)
    iterate = newton_steps(power, local_gram)
    new_basis = iterate * root_width
    return (
        new_weights[None, None],
        moment_one[None, None],
        moment_two[None, None],
        new_basis[None],
    )


def solution(mesh):
    devices = mesh.devices.reshape(mesh.shape["section"], -1, 2, mesh.shape["tensor"])
    split = Mesh(devices, ("section", "z", "core", "tensor"))
    shard = ("z", "core")
    return jax.shard_map(
        per_device,
        mesh=split,
        in_specs=(
            P("section", shard, "tensor", None),
            P("section", "tensor", shard, None),
            P("section", None, None),
            P("section", "tensor", shard, None),
            P("section", "tensor", shard, None),
        ),
        out_specs=(
            P("section", "tensor", shard, None),
            P("section", "tensor", shard, None),
            P("section", "tensor", shard, None),
            P("section", None, None),
        ),
        check_vma=False,
    )
```

```python
import math

import jax
import jax.numpy as jnp
from jax import lax
from jax.sharding import Mesh, PartitionSpec as P

NS_STEPS = 5


def matmul(left, right):
    return jnp.dot(left, right, precision=lax.Precision.HIGH, preferred_element_type=jnp.float32)


def inner_rows(left, right):
    return lax.dot_general(
        left,
        right,
        (((0,), (0,)), ((), ())),
        precision=lax.Precision.HIGH,
        preferred_element_type=jnp.float32,
    )


def local_gram(iterate):
    return inner_rows(iterate, iterate)


def newton_steps(power_part, gram_fn):
    gram_now = gram_fn(power_part)
    scaling = lax.rsqrt(jnp.trace(gram_now) + 1e-06)
    iterate = power_part * scaling
    gram_now = gram_now * (scaling * scaling)
    for sweep in range(NS_STEPS):
        iterate = 1.5 * iterate - 0.5 * matmul(iterate, gram_now)
        if sweep + 1 < NS_STEPS:
            gram_now = gram_fn(iterate)
    return iterate


def swap_cores(x):
    return lax.ppermute(x, "core", [(0, 1), (1, 0)])


def place_halves(own, partner, core):
    first = jnp.where(core == 0, own, partner)
    second = jnp.where(core == 0, partner, own)
    return jnp.stack([first, second])


def per_device(grad_terms, weights, basis, first_moment, second_moment):
    gradient = grad_terms[0, 0]
    basis_now = basis[0]
    root_width = math.sqrt(basis_now.shape[0])
    rows = first_moment.shape[2]
    n_z = lax.axis_size("z")
    core = lax.axis_index("core")
    partial = matmul(gradient, basis_now).reshape(n_z, 2, rows, -1)
    own = lax.dynamic_index_in_dim(partial, core, axis=1, keepdims=False)
    other = lax.dynamic_index_in_dim(partial, 1 - core, axis=1, keepdims=False)
    chip_sum = own + swap_cores(other)
    low_rank = lax.all_to_all(chip_sum, "z", 0, 0, tiled=True).sum(axis=0) / root_width
    gathered = lax.all_to_all(jnp.broadcast_to(low_rank[None], (n_z,) + low_rank.shape), "z", 0, 0, tiled=True)
    low_rank_block = place_halves(gathered, swap_cores(gathered), core)
    low_rank_block = jnp.moveaxis(low_rank_block, 0, 1).reshape(gradient.shape[0], -1)
    power_part = inner_rows(gradient, low_rank_block)
    n_group = n_z * lax.axis_size("tensor")
    halves = power_part.reshape(2, n_group, -1, power_part.shape[1])
    own_half = lax.dynamic_index_in_dim(halves, core, axis=0, keepdims=False)
    other_half = lax.dynamic_index_in_dim(halves, 1 - core, axis=0, keepdims=False)
    chip_half = own_half + swap_cores(other_half)
    piece = lax.all_to_all(chip_half, ("z", "tensor"), 0, 0, tiled=True).sum(axis=0)
    half = lax.all_to_all(jnp.broadcast_to(piece[None], chip_half.shape), ("z", "tensor"), 0, 0, tiled=True)
    power = place_halves(half, swap_cores(half), core).reshape(power_part.shape)
    moment_one = 0.9 * first_moment[0, 0] + 0.1 * low_rank
    moment_two = 0.95 * second_moment[0, 0] + 0.05 * low_rank * low_rank
    direction = moment_one / (jnp.sqrt(moment_two) + 1e-08)
    update = lax.dot_general(
        direction,
        basis_now,
        (((1,), (1,)), ((), ())),
        precision=lax.Precision.HIGH,
        preferred_element_type=jnp.float32,
    )
    stepped = weights[0, 0].astype(jnp.float32) - 0.5 * update / root_width
    normed = stepped * lax.rsqrt(jnp.mean(stepped * stepped, axis=1, keepdims=True) + 1e-06)
    new_weights = normed.astype(jnp.bfloat16)
    iterate = newton_steps(power, local_gram)
    new_basis = iterate * root_width
    return (
        new_weights[None, None],
        moment_one[None, None],
        moment_two[None, None],
        new_basis[None],
    )


def solution(mesh):
    devices = mesh.devices.reshape(mesh.shape["section"], -1, 2, mesh.shape["tensor"])
    split = Mesh(devices, ("section", "z", "core", "tensor"))
    shard = ("z", "core")
    return jax.shard_map(
        per_device,
        mesh=split,
        in_specs=(
            P("section", shard, "tensor", None),
            P("section", "tensor", shard, None),
            P("section", None, None),
            P("section", "tensor", shard, None),
            P("section", "tensor", shard, None),
        ),
        out_specs=(
            P("section", "tensor", shard, None),
            P("section", "tensor", shard, None),
            P("section", "tensor", shard, None),
            P("section", None, None),
        ),
        check_vma=False,
    )
```

```python
import math

import jax
import jax.numpy as jnp
from jax import lax
from jax.sharding import Mesh, PartitionSpec as P

NS_STEPS = 5


def matmul(left, right):
    return jnp.dot(left, right, precision=lax.Precision.HIGH, preferred_element_type=jnp.float32)


def inner_rows(left, right):
    return lax.dot_general(
        left,
        right,
        (((0,), (0,)), ((), ())),
        precision=lax.Precision.HIGH,
        preferred_element_type=jnp.float32,
    )


def local_gram(iterate):
    return inner_rows(iterate, iterate)


def newton_steps(power_part, gram_fn):
    gram_now = gram_fn(power_part)
    scaling = lax.rsqrt(jnp.trace(gram_now) + 1e-06)
    iterate = power_part * scaling
    gram_now = gram_now * (scaling * scaling)
    for sweep in range(NS_STEPS):
        iterate = 1.5 * iterate - 0.5 * matmul(iterate, gram_now)
        if sweep + 1 < NS_STEPS:
            gram_now = gram_fn(iterate)
    return iterate


def swap_cores(x):
    return lax.ppermute(x, "core", [(0, 1), (1, 0)])


def place_halves(own, partner, core):
    first = jnp.where(core == 0, own, partner)
    second = jnp.where(core == 0, partner, own)
    return jnp.stack([first, second])


def per_device(grad_terms, weights, basis, first_moment, second_moment):
    gradient = grad_terms[0, 0]
    basis_now = basis[0]
    root_width = math.sqrt(basis_now.shape[0])
    rows = first_moment.shape[2]
    n_z = lax.axis_size("z")
    core = lax.axis_index("core")
    partial = matmul(gradient, basis_now).reshape(n_z, 2, rows, -1)
    own = lax.dynamic_index_in_dim(partial, core, axis=1, keepdims=False)
    other = lax.dynamic_index_in_dim(partial, 1 - core, axis=1, keepdims=False)
    chip_sum = own + swap_cores(other)
    low_rank = lax.all_to_all(chip_sum, "z", 0, 0, tiled=True).sum(axis=0) / root_width
    gathered = lax.all_to_all(jnp.broadcast_to(low_rank[None], (n_z,) + low_rank.shape), "z", 0, 0, tiled=True)
    low_rank_block = place_halves(gathered, swap_cores(gathered), core)
    low_rank_block = jnp.moveaxis(low_rank_block, 0, 1).reshape(gradient.shape[0], -1)
    power_part = inner_rows(gradient, low_rank_block)
    n_group = n_z * lax.axis_size("tensor")
    width = power_part.shape[1] // 2
    own_half = lax.dynamic_slice_in_dim(power_part, core * width, width, axis=1)
    other_half = lax.dynamic_slice_in_dim(power_part, (1 - core) * width, width, axis=1)
    chip_half = (own_half + swap_cores(other_half)).reshape(n_group, -1, width)
    piece = lax.all_to_all(chip_half, ("z", "tensor"), 0, 0, tiled=True).sum(axis=0)
    half = lax.all_to_all(jnp.broadcast_to(piece[None], chip_half.shape), ("z", "tensor"), 0, 0, tiled=True)
    half = half.reshape(-1, width)
    partner = swap_cores(half)
    power = jnp.where(core == 0, jnp.concatenate([half, partner], axis=1), jnp.concatenate([partner, half], axis=1))
    moment_one = 0.9 * first_moment[0, 0] + 0.1 * low_rank
    moment_two = 0.95 * second_moment[0, 0] + 0.05 * low_rank * low_rank
    direction = moment_one / (jnp.sqrt(moment_two) + 1e-08)
    update = lax.dot_general(
        direction,
        basis_now,
        (((1,), (1,)), ((), ())),
        precision=lax.Precision.HIGH,
        preferred_element_type=jnp.float32,
    )
    stepped = weights[0, 0].astype(jnp.float32) - 0.5 * update / root_width
    normed = stepped * lax.rsqrt(jnp.mean(stepped * stepped, axis=1, keepdims=True) + 1e-06)
    new_weights = normed.astype(jnp.bfloat16)
    iterate = newton_steps(power, local_gram)
    new_basis = iterate * root_width
    return (
        new_weights[None, None],
        moment_one[None, None],
        moment_two[None, None],
        new_basis[None],
    )


def solution(mesh):
    devices = mesh.devices.reshape(mesh.shape["section"], -1, 2, mesh.shape["tensor"])
    split = Mesh(devices, ("section", "z", "core", "tensor"))
    shard = ("z", "core")
    return jax.shard_map(
        per_device,
        mesh=split,
        in_specs=(
            P("section", shard, "tensor", None),
            P("section", "tensor", shard, None),
            P("section", None, None),
            P("section", "tensor", shard, None),
            P("section", "tensor", shard, None),
        ),
        out_specs=(
            P("section", "tensor", shard, None),
            P("section", "tensor", shard, None),
            P("section", "tensor", shard, None),
            P("section", None, None),
        ),
        check_vma=False,
    )
```

```python
import math

import jax
import jax.numpy as jnp
from jax import lax
from jax.sharding import Mesh, PartitionSpec as P

NS_STEPS = 5


def matmul(left, right):
    return jnp.dot(left, right, precision=lax.Precision.HIGH, preferred_element_type=jnp.float32)


def inner_rows(left, right):
    return lax.dot_general(
        left,
        right,
        (((0,), (0,)), ((), ())),
        precision=lax.Precision.HIGH,
        preferred_element_type=jnp.float32,
    )


def local_gram(iterate):
    return inner_rows(iterate, iterate)


def newton_steps(power_part, gram_fn):
    gram_now = gram_fn(power_part)
    scaling = lax.rsqrt(jnp.trace(gram_now) + 1e-06)
    gram_now = gram_now * (scaling * scaling)
    eye = jnp.eye(gram_now.shape[0], dtype=gram_now.dtype)
    product = None
    for sweep in range(NS_STEPS):
        step = 1.5 * eye - 0.5 * gram_now
        product = step if product is None else matmul(product, step)
        if sweep + 1 < NS_STEPS:
            gram_now = inner_rows(step, matmul(gram_now, step))
    return matmul(power_part * scaling, product)


def swap_cores(x):
    return lax.ppermute(x, "core", [(0, 1), (1, 0)])


def place_halves(own, partner, core):
    first = jnp.where(core == 0, own, partner)
    second = jnp.where(core == 0, partner, own)
    return jnp.stack([first, second])


def per_device(grad_terms, weights, basis, first_moment, second_moment):
    gradient = grad_terms[0, 0]
    basis_now = basis[0]
    root_width = math.sqrt(basis_now.shape[0])
    rows = first_moment.shape[2]
    n_z = lax.axis_size("z")
    core = lax.axis_index("core")
    partial = matmul(gradient, basis_now).reshape(n_z, 2, rows, -1)
    own = lax.dynamic_index_in_dim(partial, core, axis=1, keepdims=False)
    other = lax.dynamic_index_in_dim(partial, 1 - core, axis=1, keepdims=False)
    chip_sum = own + swap_cores(other)
    low_rank = lax.all_to_all(chip_sum, "z", 0, 0, tiled=True).sum(axis=0) / root_width
    gathered = lax.all_to_all(jnp.broadcast_to(low_rank[None], (n_z,) + low_rank.shape), "z", 0, 0, tiled=True)
    low_rank_block = place_halves(gathered, swap_cores(gathered), core)
    low_rank_block = jnp.moveaxis(low_rank_block, 0, 1).reshape(gradient.shape[0], -1)
    power_part = inner_rows(gradient, low_rank_block)
    n_group = n_z * lax.axis_size("tensor")
    width = power_part.shape[1] // 2
    own_half = lax.dynamic_slice_in_dim(power_part, core * width, width, axis=1)
    other_half = lax.dynamic_slice_in_dim(power_part, (1 - core) * width, width, axis=1)
    chip_half = (own_half + swap_cores(other_half)).reshape(n_group, -1, width)
    piece = lax.all_to_all(chip_half, ("z", "tensor"), 0, 0, tiled=True).sum(axis=0)
    half = lax.all_to_all(jnp.broadcast_to(piece[None], chip_half.shape), ("z", "tensor"), 0, 0, tiled=True)
    half = half.reshape(-1, width)
    partner = swap_cores(half)
    power = jnp.where(core == 0, jnp.concatenate([half, partner], axis=1), jnp.concatenate([partner, half], axis=1))
    moment_one = 0.9 * first_moment[0, 0] + 0.1 * low_rank
    moment_two = 0.95 * second_moment[0, 0] + 0.05 * low_rank * low_rank
    direction = moment_one / (jnp.sqrt(moment_two) + 1e-08)
    update = lax.dot_general(
        direction,
        basis_now,
        (((1,), (1,)), ((), ())),
        precision=lax.Precision.HIGH,
        preferred_element_type=jnp.float32,
    )
    stepped = weights[0, 0].astype(jnp.float32) - 0.5 * update / root_width
    normed = stepped * lax.rsqrt(jnp.mean(stepped * stepped, axis=1, keepdims=True) + 1e-06)
    new_weights = normed.astype(jnp.bfloat16)
    iterate = newton_steps(power, local_gram)
    new_basis = iterate * root_width
    return (
        new_weights[None, None],
        moment_one[None, None],
        moment_two[None, None],
        new_basis[None],
    )


def solution(mesh):
    devices = mesh.devices.reshape(mesh.shape["section"], -1, 2, mesh.shape["tensor"])
    split = Mesh(devices, ("section", "z", "core", "tensor"))
    shard = ("z", "core")
    return jax.shard_map(
        per_device,
        mesh=split,
        in_specs=(
            P("section", shard, "tensor", None),
            P("section", "tensor", shard, None),
            P("section", None, None),
            P("section", "tensor", shard, None),
            P("section", "tensor", shard, None),
        ),
        out_specs=(
            P("section", "tensor", shard, None),
            P("section", "tensor", shard, None),
            P("section", "tensor", shard, None),
            P("section", None, None),
        ),
        check_vma=False,
    )
```

```python
import math

import jax
import jax.numpy as jnp
from jax import lax
from jax.sharding import Mesh, PartitionSpec as P


NS_STEPS = 5


def matmul(left, right):
    return jnp.dot(left, right, precision=lax.Precision.HIGH, preferred_element_type=jnp.float32)


def inner_rows(left, right):
    return lax.dot_general(
        left,
        right,
        (((0,), (0,)), ((), ())),
        precision=lax.Precision.HIGH,
        preferred_element_type=jnp.float32,
    )


def local_gram(iterate):
    return inner_rows(iterate, iterate)


def newton_steps(power_part, gram_fn):
    gram_now = gram_fn(power_part)
    scaling = lax.rsqrt(jnp.trace(gram_now) + 1e-06)
    gram_now = gram_now * (scaling * scaling)
    eye = jnp.eye(gram_now.shape[0], dtype=gram_now.dtype)
    product = None
    for sweep in range(NS_STEPS):
        step = 1.5 * eye - 0.5 * gram_now
        product = step if product is None else matmul(product, step)
        if sweep + 1 < NS_STEPS:
            gram_now = inner_rows(step, matmul(gram_now, step))
    return matmul(power_part * scaling, product)


def swap_cores(x):
    return lax.ppermute(x, "core", [(0, 1), (1, 0)])


def place_halves(own, partner, core):
    first = jnp.where(core == 0, own, partner)
    second = jnp.where(core == 0, partner, own)
    return jnp.stack([first, second])


def per_device(grad_terms, weights, basis, first_moment, second_moment):
    gradient = grad_terms[0, 0]
    basis_now = basis[0]
    root_width = math.sqrt(basis_now.shape[0])
    rows = first_moment.shape[2]
    n_z = lax.axis_size("z")
    core = lax.axis_index("core")
    by_core = gradient.reshape(n_z, 2, rows, -1)
    other = matmul(lax.dynamic_index_in_dim(by_core, 1 - core, axis=1, keepdims=False), basis_now)
    sent = swap_cores(other)
    own = lax.optimization_barrier(matmul(lax.dynamic_index_in_dim(by_core, core, axis=1, keepdims=False), basis_now))
    chip_sum = own + sent
    low_rank = lax.all_to_all(chip_sum, "z", 0, 0, tiled=True).sum(axis=0) / root_width
    gathered = lax.all_to_all(jnp.broadcast_to(low_rank[None], (n_z,) + low_rank.shape), "z", 0, 0, tiled=True)
    low_rank_block = place_halves(gathered, swap_cores(gathered), core)
    low_rank_block = jnp.moveaxis(low_rank_block, 0, 1).reshape(gradient.shape[0], -1)
    width = low_rank_block.shape[1] // 2
    other_cols = lax.dynamic_slice_in_dim(low_rank_block, (1 - core) * width, width, axis=1)
    own_cols = lax.dynamic_slice_in_dim(low_rank_block, core * width, width, axis=1)
    sent_half = swap_cores(inner_rows(gradient, other_cols))
    own_half = lax.optimization_barrier(inner_rows(gradient, own_cols))
    n_group = n_z * lax.axis_size("tensor")
    chip_half = (own_half + sent_half).reshape(n_group, -1, width)
    piece = lax.all_to_all(chip_half, ("z", "tensor"), 0, 0, tiled=True).sum(axis=0)
    half = lax.all_to_all(jnp.broadcast_to(piece[None], chip_half.shape), ("z", "tensor"), 0, 0, tiled=True)
    half = half.reshape(-1, width)
    partner = swap_cores(half)
    power = jnp.where(core == 0, jnp.concatenate([half, partner], axis=1), jnp.concatenate([partner, half], axis=1))
    moment_one = 0.9 * first_moment[0, 0] + 0.1 * low_rank
    moment_two = 0.95 * second_moment[0, 0] + 0.05 * low_rank * low_rank
    direction = moment_one / (jnp.sqrt(moment_two) + 1e-08)
    update = lax.dot_general(
        direction,
        basis_now,
        (((1,), (1,)), ((), ())),
        precision=lax.Precision.HIGH,
        preferred_element_type=jnp.float32,
    )
    stepped = weights[0, 0].astype(jnp.float32) - 0.5 * update / root_width
    normed = stepped * lax.rsqrt(jnp.mean(stepped * stepped, axis=1, keepdims=True) + 1e-06)
    new_weights = normed.astype(jnp.bfloat16)
    iterate = newton_steps(power, local_gram)
    new_basis = iterate * root_width
    return (
        new_weights[None, None],
        moment_one[None, None],
        moment_two[None, None],
        new_basis[None],
    )


def solution(mesh):
    devices = mesh.devices.reshape(mesh.shape["section"], -1, 2, mesh.shape["tensor"])
    split = Mesh(devices, ("section", "z", "core", "tensor"))
    shard = ("z", "core")

    return jax.shard_map(
        per_device,
        mesh=split,
        in_specs=(
            P("section", shard, "tensor", None),
            P("section", "tensor", shard, None),
            P("section", None, None),
            P("section", "tensor", shard, None),
            P("section", "tensor", shard, None),
        ),
        out_specs=(
            P("section", "tensor", shard, None),
            P("section", "tensor", shard, None),
            P("section", "tensor", shard, None),
            P("section", None, None),
        ),
        check_vma=False,
    )
```

```python
import math

import jax
import jax.numpy as jnp
from jax import lax
from jax.sharding import Mesh, PartitionSpec as P

NS_STEPS = 5


def matmul(left, right):
    return jnp.dot(left, right, precision=lax.Precision.HIGH, preferred_element_type=jnp.float32)


def inner_rows(left, right):
    return lax.dot_general(
        left,
        right,
        (((0,), (0,)), ((), ())),
        precision=lax.Precision.HIGH,
        preferred_element_type=jnp.float32,
    )


def local_gram(iterate):
    return inner_rows(iterate, iterate)


def newton_steps(power_part, gram_fn):
    gram_now = gram_fn(power_part)
    scaling = lax.rsqrt(jnp.trace(gram_now) + 1e-06)
    gram_now = gram_now * (scaling * scaling)
    eye = jnp.eye(gram_now.shape[0], dtype=gram_now.dtype)
    product = None
    for sweep in range(NS_STEPS):
        step = 1.5 * eye - 0.5 * gram_now
        product = step if product is None else matmul(product, step)
        if sweep + 1 < NS_STEPS:
            gram_now = inner_rows(step, matmul(gram_now, step))
    return matmul(power_part * scaling, product)


def swap_cores(x):
    return lax.ppermute(x, "core", [(0, 1), (1, 0)])


def place_halves(own, partner, core):
    first = jnp.where(core == 0, own, partner)
    second = jnp.where(core == 0, partner, own)
    return jnp.stack([first, second])


def per_device(grad_terms, weights, basis, first_moment, second_moment):
    gradient = grad_terms[0, 0]
    basis_now = basis[0]
    root_width = math.sqrt(basis_now.shape[0])
    rows = first_moment.shape[2]
    n_z = lax.axis_size("z")
    core = lax.axis_index("core")
    by_core = gradient.reshape(n_z, 2, rows, -1)
    other = matmul(lax.dynamic_index_in_dim(by_core, 1 - core, axis=1, keepdims=False), basis_now)
    sent = swap_cores(other)
    own = lax.optimization_barrier(matmul(lax.dynamic_index_in_dim(by_core, core, axis=1, keepdims=False), basis_now))
    chip_sum = own + sent
    low_rank = lax.all_to_all(chip_sum, "z", 0, 0, tiled=True).sum(axis=0) / root_width
    gathered = lax.all_to_all(jnp.broadcast_to(low_rank[None], (n_z,) + low_rank.shape), "z", 0, 0, tiled=True)
    low_rank_block = place_halves(gathered, swap_cores(gathered), core)
    low_rank_block = jnp.moveaxis(low_rank_block, 0, 1).reshape(gradient.shape[0], -1)
    power_part = inner_rows(gradient, low_rank_block)
    n_group = n_z * lax.axis_size("tensor")
    width = power_part.shape[1] // 2
    own_half = lax.dynamic_slice_in_dim(power_part, core * width, width, axis=1)
    other_half = lax.dynamic_slice_in_dim(power_part, (1 - core) * width, width, axis=1)
    chip_half = (own_half + swap_cores(other_half)).reshape(n_group, -1, width)
    piece = lax.all_to_all(chip_half, ("z", "tensor"), 0, 0, tiled=True).sum(axis=0)
    half = lax.all_to_all(jnp.broadcast_to(piece[None], chip_half.shape), ("z", "tensor"), 0, 0, tiled=True)
    half = half.reshape(-1, width)
    partner = swap_cores(half)
    power = jnp.where(core == 0, jnp.concatenate([half, partner], axis=1), jnp.concatenate([partner, half], axis=1))
    moment_one = 0.9 * first_moment[0, 0] + 0.1 * low_rank
    moment_two = 0.95 * second_moment[0, 0] + 0.05 * low_rank * low_rank
    direction = moment_one / (jnp.sqrt(moment_two) + 1e-08)
    update = lax.dot_general(
        direction,
        basis_now,
        (((1,), (1,)), ((), ())),
        precision=lax.Precision.HIGH,
        preferred_element_type=jnp.float32,
    )
    stepped = weights[0, 0].astype(jnp.float32) - 0.5 * update / root_width
    normed = stepped * lax.rsqrt(jnp.mean(stepped * stepped, axis=1, keepdims=True) + 1e-06)
    new_weights = normed.astype(jnp.bfloat16)
    iterate = newton_steps(power, local_gram)
    new_basis = iterate * root_width
    return (
        new_weights[None, None],
        moment_one[None, None],
        moment_two[None, None],
        new_basis[None],
    )


def solution(mesh):
    devices = mesh.devices.reshape(mesh.shape["section"], -1, 2, mesh.shape["tensor"])
    split = Mesh(devices, ("section", "z", "core", "tensor"))
    shard = ("z", "core")
    return jax.shard_map(
        per_device,
        mesh=split,
        in_specs=(
            P("section", shard, "tensor", None),
            P("section", "tensor", shard, None),
            P("section", None, None),
            P("section", "tensor", shard, None),
            P("section", "tensor", shard, None),
        ),
        out_specs=(
            P("section", "tensor", shard, None),
            P("section", "tensor", shard, None),
            P("section", "tensor", shard, None),
            P("section", None, None),
        ),
        check_vma=False,
    )
```

```python
import math

import jax
import jax.numpy as jnp
from jax import lax
from jax.sharding import Mesh, PartitionSpec as P

NS_STEPS = 5


def matmul(left, right):
    return jnp.dot(left, right, precision=lax.Precision.HIGH, preferred_element_type=jnp.float32)


def inner_rows(left, right):
    return lax.dot_general(
        left,
        right,
        (((0,), (0,)), ((), ())),
        precision=lax.Precision.HIGH,
        preferred_element_type=jnp.float32,
    )


def local_gram(iterate):
    return inner_rows(iterate, iterate)


def newton_steps(power_part, gram_fn):
    gram_now = gram_fn(power_part)
    scaling = lax.rsqrt(jnp.trace(gram_now) + 1e-06)
    gram_now = gram_now * (scaling * scaling)
    eye = jnp.eye(gram_now.shape[0], dtype=gram_now.dtype)
    product = None
    for sweep in range(NS_STEPS):
        step = 1.5 * eye - 0.5 * gram_now
        product = step if product is None else matmul(product, step)
        if sweep + 1 < NS_STEPS:
            gram_now = inner_rows(step, matmul(gram_now, step))
    return matmul(power_part * scaling, product)


def swap_cores(x):
    return lax.ppermute(x, "core", [(0, 1), (1, 0)])


def place_halves(own, partner, core):
    first = jnp.where(core == 0, own, partner)
    second = jnp.where(core == 0, partner, own)
    return jnp.stack([first, second])


def per_device(grad_terms, weights, basis, first_moment, second_moment):
    gradient = grad_terms[0, 0]
    basis_now = basis[0]
    root_width = math.sqrt(basis_now.shape[0])
    rows = first_moment.shape[2]
    n_z = lax.axis_size("z")
    core = lax.axis_index("core")
    partial = matmul(gradient, basis_now).reshape(n_z, 2, rows, -1)
    own = lax.dynamic_index_in_dim(partial, core, axis=1, keepdims=False)
    other = lax.dynamic_index_in_dim(partial, 1 - core, axis=1, keepdims=False)
    chip_sum = own + swap_cores(other)
    low_rank = lax.all_to_all(chip_sum, "z", 0, 0, tiled=True).sum(axis=0) / root_width
    low_rank_block = lax.all_to_all(
        jnp.broadcast_to(low_rank[None], (2 * n_z,) + low_rank.shape), ("z", "core"), 0, 0, tiled=True
    ).reshape(gradient.shape[0], -1)
    power_part = inner_rows(gradient, low_rank_block)
    n_group = n_z * lax.axis_size("tensor")
    width = power_part.shape[1] // 2
    own_half = lax.dynamic_slice_in_dim(power_part, core * width, width, axis=1)
    other_half = lax.dynamic_slice_in_dim(power_part, (1 - core) * width, width, axis=1)
    chip_half = (own_half + swap_cores(other_half)).reshape(n_group, -1, width)
    piece = lax.all_to_all(chip_half, ("z", "tensor"), 0, 0, tiled=True).sum(axis=0)
    half = lax.all_to_all(jnp.broadcast_to(piece[None], chip_half.shape), ("z", "tensor"), 0, 0, tiled=True)
    half = half.reshape(-1, width)
    partner = swap_cores(half)
    power = jnp.where(core == 0, jnp.concatenate([half, partner], axis=1), jnp.concatenate([partner, half], axis=1))
    moment_one = 0.9 * first_moment[0, 0] + 0.1 * low_rank
    moment_two = 0.95 * second_moment[0, 0] + 0.05 * low_rank * low_rank
    direction = moment_one / (jnp.sqrt(moment_two) + 1e-08)
    update = lax.dot_general(
        direction,
        basis_now,
        (((1,), (1,)), ((), ())),
        precision=lax.Precision.HIGH,
        preferred_element_type=jnp.float32,
    )
    stepped = weights[0, 0].astype(jnp.float32) - 0.5 * update / root_width
    normed = stepped * lax.rsqrt(jnp.mean(stepped * stepped, axis=1, keepdims=True) + 1e-06)
    new_weights = normed.astype(jnp.bfloat16)
    iterate = newton_steps(power, local_gram)
    new_basis = iterate * root_width
    return (
        new_weights[None, None],
        moment_one[None, None],
        moment_two[None, None],
        new_basis[None],
    )


def solution(mesh):
    devices = mesh.devices.reshape(mesh.shape["section"], -1, 2, mesh.shape["tensor"])
    split = Mesh(devices, ("section", "z", "core", "tensor"))
    shard = ("z", "core")
    return jax.shard_map(
        per_device,
        mesh=split,
        in_specs=(
            P("section", shard, "tensor", None),
            P("section", "tensor", shard, None),
            P("section", None, None),
            P("section", "tensor", shard, None),
            P("section", "tensor", shard, None),
        ),
        out_specs=(
            P("section", "tensor", shard, None),
            P("section", "tensor", shard, None),
            P("section", "tensor", shard, None),
            P("section", None, None),
        ),
        check_vma=False,
    )
```

```python
import math

import jax
import jax.numpy as jnp
from jax import lax
from jax.sharding import Mesh, PartitionSpec as P

NS_STEPS = 5


def matmul(left, right):
    return jnp.dot(left, right, precision=lax.Precision.HIGH, preferred_element_type=jnp.float32)


def inner_rows(left, right):
    return lax.dot_general(
        left,
        right,
        (((0,), (0,)), ((), ())),
        precision=lax.Precision.HIGH,
        preferred_element_type=jnp.float32,
    )


def local_gram(iterate):
    return inner_rows(iterate, iterate)


def newton_steps(power_part, gram_fn):
    gram_now = gram_fn(power_part)
    scaling = lax.rsqrt(jnp.trace(gram_now) + 1e-06)
    gram_now = gram_now * (scaling * scaling)
    eye = jnp.eye(gram_now.shape[0], dtype=gram_now.dtype)
    product = None
    for sweep in range(NS_STEPS):
        step = 1.5 * eye - 0.5 * gram_now
        product = step if product is None else matmul(product, step)
        if sweep + 1 < NS_STEPS:
            gram_now = inner_rows(step, matmul(gram_now, step))
    return matmul(power_part, product * (scaling * math.sqrt(power_part.shape[0])))


def swap_cores(x):
    return lax.ppermute(x, "core", [(0, 1), (1, 0)])


def place_halves(own, partner, core):
    first = jnp.where(core == 0, own, partner)
    second = jnp.where(core == 0, partner, own)
    return jnp.stack([first, second])


def per_device(grad_terms, weights, basis, first_moment, second_moment):
    gradient = grad_terms[0, 0]
    basis_now = basis[0]
    root_width = math.sqrt(basis_now.shape[0])
    rows = first_moment.shape[2]
    n_z = lax.axis_size("z")
    core = lax.axis_index("core")
    partial = matmul(gradient, basis_now).reshape(n_z, 2, rows, -1)
    own = lax.dynamic_index_in_dim(partial, core, axis=1, keepdims=False)
    other = lax.dynamic_index_in_dim(partial, 1 - core, axis=1, keepdims=False)
    chip_sum = own + swap_cores(other)
    low_rank = lax.all_to_all(chip_sum, "z", 0, 0, tiled=True).sum(axis=0) / root_width
    gathered = lax.all_to_all(jnp.broadcast_to(low_rank[None], (n_z,) + low_rank.shape), "z", 0, 0, tiled=True)
    low_rank_block = place_halves(gathered, swap_cores(gathered), core)
    low_rank_block = jnp.moveaxis(low_rank_block, 0, 1).reshape(gradient.shape[0], -1)
    power_part = inner_rows(gradient, low_rank_block)
    n_group = n_z * lax.axis_size("tensor")
    width = power_part.shape[1] // 2
    own_half = lax.dynamic_slice_in_dim(power_part, core * width, width, axis=1)
    other_half = lax.dynamic_slice_in_dim(power_part, (1 - core) * width, width, axis=1)
    chip_half = (own_half + swap_cores(other_half)).reshape(n_group, -1, width)
    piece = lax.all_to_all(chip_half, ("z", "tensor"), 0, 0, tiled=True).sum(axis=0)
    half = lax.all_to_all(jnp.broadcast_to(piece[None], chip_half.shape), ("z", "tensor"), 0, 0, tiled=True)
    half = half.reshape(-1, width)
    partner = swap_cores(half)
    power = jnp.where(core == 0, jnp.concatenate([half, partner], axis=1), jnp.concatenate([partner, half], axis=1))
    moment_one = 0.9 * first_moment[0, 0] + 0.1 * low_rank
    moment_two = 0.95 * second_moment[0, 0] + 0.05 * low_rank * low_rank
    direction = moment_one / (jnp.sqrt(moment_two) + 1e-08)
    update = lax.dot_general(
        direction,
        basis_now,
        (((1,), (1,)), ((), ())),
        precision=lax.Precision.HIGH,
        preferred_element_type=jnp.float32,
    )
    stepped = weights[0, 0].astype(jnp.float32) - 0.5 * update / root_width
    normed = stepped * lax.rsqrt(jnp.mean(stepped * stepped, axis=1, keepdims=True) + 1e-06)
    new_weights = normed.astype(jnp.bfloat16)
    iterate = newton_steps(power, local_gram)
    new_basis = iterate
    return (
        new_weights[None, None],
        moment_one[None, None],
        moment_two[None, None],
        new_basis[None],
    )


def solution(mesh):
    devices = mesh.devices.reshape(mesh.shape["section"], -1, 2, mesh.shape["tensor"])
    split = Mesh(devices, ("section", "z", "core", "tensor"))
    shard = ("z", "core")
    return jax.shard_map(
        per_device,
        mesh=split,
        in_specs=(
            P("section", shard, "tensor", None),
            P("section", "tensor", shard, None),
            P("section", None, None),
            P("section", "tensor", shard, None),
            P("section", "tensor", shard, None),
        ),
        out_specs=(
            P("section", "tensor", shard, None),
            P("section", "tensor", shard, None),
            P("section", "tensor", shard, None),
            P("section", None, None),
        ),
        check_vma=False,
    )
```
